256 devices in a mesh: dp: 8 (over x, core), expert: 32 (over y, z).
Axes of the slice: x: 4, y: 4, z: 8, core: 2. Of those that a mesh axis runs over, the one named last changes fastest.
Arguments:
- tokens: bfloat16 [4096, 3584], P('expert'), may hold values from -6 to 6
- cotangent: bfloat16 [4096, 3584], P('expert'), may hold values from -0.59765625 to 0.59765625
- route_ids: int32 [4096, 8], P('expert'), may hold values from 0 to 31, all different within a row; in each aligned block of 128 rows (0 to 127, 128 to 255, ...) at most 40 rows name the same one
- route_gates: float32 [4096, 8], P('expert'), may hold values from 0.02 to 0.5
- w_gate: bfloat16 [32, 1792, 3584], P('expert', 'dp'), may hold values from -0.09375 to 0.09375
- w_up: bfloat16 [32, 1792, 3584], P('expert', 'dp'), may hold values from -0.09375 to 0.09375
- w_down: bfloat16 [32, 1792, 3584], P('expert', 'dp'), may hold values from -0.125 to 0.125
Outputs:
- layer_out: bfloat16 [4096, 3584], P(('expert', 'dp'))
- gate_grad: float32 [4096, 8], P(('expert', 'dp'))
- grad_w_gate: bfloat16 [32, 1792, 3584], P('expert', 'dp')
- grad_w_up: bfloat16 [32, 1792, 3584], P('expert', 'dp')
- grad_w_down: bfloat16 [32, 1792, 3584], P('expert', 'dp')
The draws below stay inside these ranges and needn't reach their ends.
Inputs may be any that keep to these rules, and one draw needn't show every extreme that they name: `route_ids`: each row names 8 different experts. Within each aligned block of 128 rows (the tokens of one index of expert) no expert is named more than 40 times, a bound that some block reaches.
All inputs are finite; a program needn't handle non-finite values.
Results may differ from the reference program's by a relative error of at most 0.02.
Values may be sent and summed in bfloat16 or wider, within the bound.
No kernel may reach another device: no remote copies, remote signals or barrier semaphores. Data moves between devices by JAX's collectives and lax.ppermute only.
A program may use at most 128 MiB of HBM per device.

```python
import math
import jax
import jax.numpy as jnp
import numpy as np
from jax import lax

D = 3584
H = 1792
TOPK = 8
TOK_GRP = 128
EXPERTS = 32
TOKENS = 4096
CAP = 40
N_DP = 8
N_EXPERT = 32


def block_levels(rng, extent, shards, least, top_value):
    factor_of = 1.0
    for axis_at, parts in shards:
        heights = jax.random.uniform(jax.random.fold_in(jax.random.fold_in(rng, 6), axis_at), (parts,), jnp.float32, least / len(shards), top_value / len(shards))
        factor_of = factor_of * jnp.repeat(jnp.exp(heights), extent[axis_at] // parts).reshape((-1,) + (1,) * (len(extent) - 1 - axis_at))
    return factor_of


def routed_block(own_key, own, number, rows, amount, top, reach, lean):
    sequence = jax.random.permutation(own_key, amount)
    heavy_load, ordinary = portions_of(amount, rows * top, reach, lean, True), portions_of(amount, rows * top, reach, lean, False)
    places = jnp.arange(amount)

    def named(lengths, offset_by):
        used = int((lengths > 0).sum())
        fixed = max(1, used // 4)
        shifted = fixed + (places - fixed + offset_by * (used - fixed)) % max(1, amount - fixed)
        return jnp.zeros((amount,), jnp.int32).at[sequence[jnp.where(places < fixed, places, shifted)]].set(jnp.asarray(lengths, jnp.int32))

    lengths = jnp.where(number % 4 == 0, named(heavy_load, number // 4), named(ordinary, number - number // 4 - 1))
    mixed = jax.random.permutation(jax.random.fold_in(own, 3), amount)
    donor, sink = mixed[0:amount // 2 * 2:2], mixed[1:amount // 2 * 2:2]
    margin = jnp.minimum(lengths[donor] - 1, reach - lengths[sink]) // 2
    margin = jnp.where((donor == sequence[0]) | (sink == sequence[0]) | (lengths[sink] == 0), 0, jnp.maximum(margin, 0))
    shifted = jax.random.randint(jax.random.fold_in(own, 4), (amount // 2,), 0, 1 << 20) % (margin + 1)
    lengths = lengths.at[donor].add(-shifted).at[sink].add(shifted)
    items = jnp.searchsorted(jnp.cumsum(lengths), jnp.arange(rows * top), side="right").astype(jnp.int32)
    grid = items.reshape(top, rows).T
    grid = grid[jax.random.permutation(jax.random.fold_in(own, 1), rows)]
    offset_by = jax.random.randint(jax.random.fold_in(own, 2), (rows, 1), 0, top)
    return jnp.take_along_axis(grid, (jnp.arange(top)[None, :] + offset_by) % top, axis=1)


def portions_of(number_of, total, reach, lean, full):
    loads = [(1 << 20) // math.isqrt(grade ** lean) + 1 for grade in range(1, number_of + 1)]
    largest = reach if full else min(reach, max(-(-total // number_of), total * loads[0] // sum(loads)))
    least = 1 if total - largest >= number_of - 1 else 0
    holding, surplus = [largest] + [least] * (number_of - 1), total - largest - least * (number_of - 1)
    while surplus > 0:
        free = [i for i in range(1, number_of) if holding[i] < largest] or [i for i in range(1, number_of) if holding[i] < reach]
        pool, budget = sum([loads[i] for i in free]), surplus
        for i in free:
            more = min(reach - holding[i], max(1, budget * loads[i] // pool), surplus)
            holding[i] = holding[i] + more
            surplus = surplus - more
    return np.array(holding)


def scatter_about(own_key, shape, scale, most, split=(), kind=jnp.bfloat16):
    result = scale * jax.random.normal(own_key, shape, jnp.float32)
    if split:
        result = result * block_levels(own_key, shape, split, -0.22, 0.18)
    return jnp.clip(result, -most, most).astype(kind)


def setup_inputs(seed: int = 0) -> dict:
    streams_of = jax.random.split(jax.random.key(seed), 8)
    tokens = scatter_about(streams_of[0], (TOKENS, D), 1.0, 6.0, ((0, 32),))
    cotangent = scatter_about(streams_of[1], (TOKENS, D), 0.1, 0.59765625, ((0, 32),))
    route_ids_keys = jax.random.split(jax.random.fold_in(streams_of[2], 1), TOKENS // TOK_GRP)
    route_ids_turns = jax.random.permutation(jax.random.fold_in(streams_of[2], 3), TOKENS // TOK_GRP)
    route_ids = jax.vmap(lambda own, number: routed_block(jax.random.fold_in(streams_of[2], 2), own, number, TOK_GRP, EXPERTS, TOPK, CAP, 2))(route_ids_keys, route_ids_turns).reshape((TOKENS, TOPK))
    route_gates = jnp.clip(jnp.exp(math.log(0.5) - 3.218876 * jax.random.uniform(streams_of[3], (TOKENS, TOPK), jnp.float32) ** block_levels(streams_of[3], (TOKENS, TOPK), ((0, 32),), -0.2, 0.2)), 0.02, 0.5)
    w_gate = scatter_about(streams_of[4], (EXPERTS, H, D), D ** -0.5, 0.09375, ((0, 32), (1, 8)))
    w_up = scatter_about(streams_of[5], (EXPERTS, H, D), D ** -0.5, 0.09375, ((0, 32), (1, 8)))
    w_down = scatter_about(streams_of[6], (EXPERTS, H, D), H ** -0.5, 0.125, ((0, 32), (1, 8)))
    return dict(tokens=tokens, cotangent=cotangent, route_ids=route_ids, route_gates=route_gates, w_gate=w_gate, w_up=w_up, w_down=w_down)


def reference(tokens, cotangent, route_ids, route_gates, w_gate, w_up, w_down):
    flat_ids = route_ids.reshape(-1)
    slot_total = flat_ids.shape[0]
    block_width = H // N_DP
    limit_rows = N_EXPERT * CAP
    rows_x = jnp.repeat(tokens, TOPK, axis=0)
    rows_cot = jnp.repeat(cotangent, TOPK, axis=0)
    scaled = (route_gates[:, :, None] * cotangent[:, None, :].astype(jnp.float32)).astype(jnp.bfloat16)
    scaled = scaled.reshape(slot_total, D)

    def per_expert(running, expert):
        y_acc, g_acc = running
        chosen = jnp.nonzero(flat_ids == expert, size=limit_rows, fill_value=slot_total)[0].astype(jnp.int32)
        rows_in = jnp.take(rows_x, chosen, axis=0, mode="fill", fill_value=0)
        rows_dy = jnp.take(scaled, chosen, axis=0, mode="fill", fill_value=0)
        rows_ct = jnp.take(rows_cot, chosen, axis=0, mode="fill", fill_value=0)
        gate_local = lax.dynamic_index_in_dim(w_gate, expert, 0, keepdims=False)
        up_local = lax.dynamic_index_in_dim(w_up, expert, 0, keepdims=False)
        down_local = lax.dynamic_index_in_dim(w_down, expert, 0, keepdims=False)
        gate_pre = jnp.dot(rows_in, gate_local.T, preferred_element_type=jnp.float32)
        up_pre = jnp.dot(rows_in, up_local.T, preferred_element_type=jnp.float32)
        sigma_gate = jax.nn.sigmoid(gate_pre)
        hidden = (gate_pre * sigma_gate * up_pre).astype(jnp.bfloat16)
        y_part = jnp.einsum(
            "rjh,jhd->rjd",
            hidden.reshape(limit_rows, N_DP, block_width).astype(jnp.float32),
            down_local.reshape(N_DP, block_width, D).astype(jnp.float32),
            precision=lax.Precision.HIGHEST,
        ).astype(jnp.bfloat16)
        y_sum = jnp.sum(y_part.astype(jnp.float32), axis=1)
        g_sum = jnp.sum(y_sum * rows_ct.astype(jnp.float32), axis=1)
        y_acc = y_acc.at[chosen].add(y_sum, mode="drop")
        g_acc = g_acc.at[chosen].add(g_sum, mode="drop")
        hidden_grad = jnp.dot(rows_dy, down_local.T, preferred_element_type=jnp.float32)
        grad_gate_pre = (hidden_grad * up_pre * sigma_gate * (1.0 + gate_pre * (1.0 - sigma_gate))).astype(jnp.bfloat16)
        grad_up_pre = (hidden_grad * gate_pre * sigma_gate).astype(jnp.bfloat16)
        grad_down = jnp.dot(hidden.T, rows_dy, preferred_element_type=jnp.float32).astype(jnp.bfloat16)
        grad_gate = jnp.dot(grad_gate_pre.T, rows_in, preferred_element_type=jnp.float32).astype(jnp.bfloat16)
        grad_up = jnp.dot(grad_up_pre.T, rows_in, preferred_element_type=jnp.float32).astype(jnp.bfloat16)
        return (y_acc, g_acc), (grad_gate, grad_up, grad_down)

    start_state = (jnp.zeros((slot_total, D), jnp.float32), jnp.zeros((slot_total,), jnp.float32))
    final_state, grads = lax.scan(per_expert, start_state, jnp.arange(N_EXPERT, dtype=jnp.int32))
    y_all, g_all = final_state
    y_tok = y_all.reshape(TOKENS, TOPK, D)
    layer_out = jnp.sum(route_gates[:, :, None] * y_tok, axis=1).astype(jnp.bfloat16)
    gate_grad = g_all.reshape(TOKENS, TOPK)
    return layer_out, gate_grad, grads[0], grads[1], grads[2]
```

```python
import jax
import jax.numpy as jnp
from jax import lax
from jax.sharding import PartitionSpec as P


def body(tokens, cotangent, route_ids, route_gates, w_gate, w_up, w_down):
    groups = lax.axis_size("expert")
    dp_count = lax.axis_size("dp")
    dp_idx = lax.axis_index("dp")
    tok_rows, width = tokens.shape
    top_slots = route_ids.shape[1]
    cap_rows = min(tok_rows, dp_count * max(1, tok_rows * top_slots * 5 // (4 * groups * dp_count)))
    share = cap_rows // dp_count
    n_dest = groups * share
    flat_ids = route_ids.reshape(-1)
    onehot = (flat_ids[:, None] == jnp.arange(groups, dtype=jnp.int32)[None, :]).astype(jnp.int32)
    slot_rank = jnp.sum(jnp.cumsum(onehot, axis=0) * onehot, axis=1) - 1
    local_rank = slot_rank - dp_idx * share
    mine = (local_rank >= 0) & (local_rank < share)
    dest = jnp.where(mine, flat_ids * share + local_rank, n_dest)
    dest_hot = (dest[:, None] == jnp.arange(n_dest, dtype=jnp.int32)[None, :]).astype(jnp.float32)
    pick = jnp.sum(dest_hot.reshape(tok_rows, top_slots, n_dest), axis=1).T
    pick_bf = pick.astype(jnp.bfloat16)
    gate_sel = jnp.sum(dest_hot * route_gates.reshape(-1)[:, None], axis=0)
    send_x = jnp.dot(pick_bf, tokens, preferred_element_type=jnp.float32).astype(jnp.bfloat16)
    cot_sel = jnp.dot(pick_bf, cotangent, preferred_element_type=jnp.float32)
    send_dy = (gate_sel[:, None] * cot_sel).astype(jnp.bfloat16)
    recv_x = lax.all_to_all(
        send_x.reshape(groups, share, width), "expert", split_axis=0, concat_axis=0, tiled=True
    )
    recv_dy = lax.all_to_all(
        send_dy.reshape(groups, share, width), "expert", split_axis=0, concat_axis=0, tiled=True
    )
    rows_all = dp_count * groups * share
    flat_x = lax.all_gather(recv_x, "dp", axis=0, tiled=False).reshape(rows_all, width)
    flat_dy = lax.all_gather(recv_dy, "dp", axis=0, tiled=False).reshape(rows_all, width)
    gate_local = w_gate[0]
    up_local = w_up[0]
    down_local = w_down[0]
    by_feature = (((1,), (1,)), ((), ()))
    by_row = (((0,), (0,)), ((), ()))
    gate_pre = lax.dot_general(flat_x, gate_local, by_feature, preferred_element_type=jnp.float32)
    up_pre = lax.dot_general(flat_x, up_local, by_feature, preferred_element_type=jnp.float32)
    sigma_gate = jax.nn.sigmoid(gate_pre)
    hidden = (gate_pre * sigma_gate * up_pre).astype(jnp.bfloat16)
    y_part = jnp.dot(hidden, down_local, preferred_element_type=jnp.float32).astype(jnp.bfloat16)
    hidden_grad = lax.dot_general(
        flat_dy, down_local, by_feature, preferred_element_type=jnp.float32
    )
    grad_gate_pre = (
        hidden_grad * up_pre * sigma_gate * (1.0 + gate_pre * (1.0 - sigma_gate))
    ).astype(jnp.bfloat16)
    grad_up_pre = (hidden_grad * gate_pre * sigma_gate).astype(jnp.bfloat16)
    grad_down = lax.dot_general(hidden, flat_dy, by_row, preferred_element_type=jnp.float32)
    grad_gate = lax.dot_general(grad_gate_pre, flat_x, by_row, preferred_element_type=jnp.float32)
    grad_up = lax.dot_general(grad_up_pre, flat_x, by_row, preferred_element_type=jnp.float32)
    y_sum = lax.psum_scatter(
        y_part.astype(jnp.float32).reshape(dp_count, groups * share, width),
        "dp",
        scatter_dimension=0,
        tiled=False,
    )
    y_home = lax.all_to_all(
        y_sum.reshape(groups, share, width), "expert", split_axis=0, concat_axis=0, tiled=True
    ).reshape(n_dest, width)
    out_part = lax.dot_general(
        pick,
        gate_sel[:, None] * y_home,
        by_row,
        precision=lax.Precision.HIGHEST,
        preferred_element_type=jnp.float32,
    )
    dot_dest = jnp.sum(cot_sel * y_home, axis=1)
    dot_ext = jnp.concatenate([dot_dest, jnp.zeros((1,), jnp.float32)])
    grad_part = dot_ext[dest].reshape(tok_rows, top_slots)
    layer_sum = lax.psum_scatter(out_part, "dp", scatter_dimension=0, tiled=True)
    gate_sum = lax.psum_scatter(grad_part, "dp", scatter_dimension=0, tiled=True)
    return (
        layer_sum.astype(jnp.bfloat16),
        gate_sum,
        grad_gate.astype(jnp.bfloat16)[None],
        grad_up.astype(jnp.bfloat16)[None],
        grad_down.astype(jnp.bfloat16)[None],
    )


def solution(mesh):
    return jax.shard_map(
        body,
        mesh=mesh,
        in_specs=(
            P("expert", None),
            P("expert", None),
            P("expert", None),
            P("expert", None),
            P("expert", "dp", None),
            P("expert", "dp", None),
            P("expert", "dp", None),
        ),
        out_specs=(
            P(("expert", "dp"), None),
            P(("expert", "dp"), None),
            P("expert", "dp", None),
            P("expert", "dp", None),
            P("expert", "dp", None),
        ),
        check_vma=False,
    )
```

```python
import jax
import jax.numpy as jnp
from jax import lax
from jax.sharding import PartitionSpec as P


def body(tokens, cotangent, route_ids, route_gates, w_gate, w_up, w_down):
    groups = lax.axis_size("expert")
    dp_count = lax.axis_size("dp")
    dp_idx = lax.axis_index("dp")
    tok_rows, width = tokens.shape
    top_slots = route_ids.shape[1]
    cap_rows = min(tok_rows, dp_count * max(1, tok_rows * top_slots * 5 // (4 * groups * dp_count)))
    share = cap_rows // dp_count
    n_dest = groups * share
    flat_ids = route_ids.reshape(-1)
    onehot = (flat_ids[:, None] == jnp.arange(groups, dtype=jnp.int32)[None, :]).astype(jnp.int32)
    slot_rank = jnp.sum(jnp.cumsum(onehot, axis=0) * onehot, axis=1) - 1
    local_rank = slot_rank - dp_idx * share
    mine = (local_rank >= 0) & (local_rank < share)
    dest = jnp.where(mine, local_rank * groups + flat_ids, n_dest)
    dest_hot = (dest[:, None] == jnp.arange(n_dest, dtype=jnp.int32)[None, :]).astype(jnp.float32)
    pick = jnp.sum(dest_hot.reshape(tok_rows, top_slots, n_dest), axis=1).T
    pick_bf = pick.astype(jnp.bfloat16)
    gate_sel = jnp.sum(dest_hot * route_gates.reshape(-1)[:, None], axis=0)
    send_x = jnp.dot(pick_bf, tokens, preferred_element_type=jnp.float32).astype(jnp.bfloat16)
    cot_sel = jnp.dot(pick_bf, cotangent, preferred_element_type=jnp.float32)
    send_dy = (gate_sel[:, None] * cot_sel).astype(jnp.bfloat16)

    def to_lanes(rows):
        return jnp.concatenate(
            [rows[r * groups : (r + 1) * groups] for r in range(share)], axis=1
        )

    def lanes_to_rows(packed):
        return jnp.concatenate(
            [packed[:, r * width : (r + 1) * width] for r in range(share)], axis=0
        )

    recv_x = lax.all_to_all(to_lanes(send_x), "expert", split_axis=0, concat_axis=0, tiled=True)
    recv_dy = lax.all_to_all(to_lanes(send_dy), "expert", split_axis=0, concat_axis=0, tiled=True)
    flat_x = lanes_to_rows(lax.all_gather(recv_x, "dp", axis=0, tiled=True))
    flat_dy = lanes_to_rows(lax.all_gather(recv_dy, "dp", axis=0, tiled=True))
    gate_local = w_gate[0]
    up_local = w_up[0]
    down_local = w_down[0]
    by_feature = (((1,), (1,)), ((), ()))
    by_row = (((0,), (0,)), ((), ()))
    gate_pre = lax.dot_general(flat_x, gate_local, by_feature, preferred_element_type=jnp.float32)
    up_pre = lax.dot_general(flat_x, up_local, by_feature, preferred_element_type=jnp.float32)
    sigma_gate = jax.nn.sigmoid(gate_pre)
    hidden = (gate_pre * sigma_gate * up_pre).astype(jnp.bfloat16)
    y_part = jnp.dot(hidden, down_local, preferred_element_type=jnp.float32).astype(jnp.bfloat16)
    hidden_grad = lax.dot_general(
        flat_dy, down_local, by_feature, preferred_element_type=jnp.float32
    )
    grad_gate_pre = (
        hidden_grad * up_pre * sigma_gate * (1.0 + gate_pre * (1.0 - sigma_gate))
    ).astype(jnp.bfloat16)
    grad_up_pre = (hidden_grad * gate_pre * sigma_gate).astype(jnp.bfloat16)
    grad_down = lax.dot_general(hidden, flat_dy, by_row, preferred_element_type=jnp.float32)
    grad_gate = lax.dot_general(grad_gate_pre, flat_x, by_row, preferred_element_type=jnp.float32)
    grad_up = lax.dot_general(grad_up_pre, flat_x, by_row, preferred_element_type=jnp.float32)
    stack_rows = dp_count * groups
    y_lanes = jnp.concatenate(
        [y_part[r * stack_rows : (r + 1) * stack_rows] for r in range(share)], axis=1
    )
    y_sum = lax.psum_scatter(y_lanes, "dp", scatter_dimension=0, tiled=True)
    y_back = lax.all_to_all(y_sum, "expert", split_axis=0, concat_axis=0, tiled=True)
    y_home = lanes_to_rows(y_back).astype(jnp.float32)
    out_part = lax.dot_general(
        pick,
        gate_sel[:, None] * y_home,
        by_row,
        precision=lax.Precision.HIGHEST,
        preferred_element_type=jnp.float32,
    )
    dot_dest = jnp.sum(cot_sel * y_home, axis=1)
    dot_ext = jnp.concatenate([dot_dest, jnp.zeros((1,), jnp.float32)])
    grad_part = dot_ext[dest].reshape(tok_rows, top_slots)
    layer_sum = lax.psum_scatter(out_part, "dp", scatter_dimension=0, tiled=True)
    gate_sum = lax.psum_scatter(grad_part, "dp", scatter_dimension=0, tiled=True)
    return (
        layer_sum.astype(jnp.bfloat16),
        gate_sum,
        grad_gate.astype(jnp.bfloat16)[None],
        grad_up.astype(jnp.bfloat16)[None],
        grad_down.astype(jnp.bfloat16)[None],
    )


def solution(mesh):
    return jax.shard_map(
        body,
        mesh=mesh,
        in_specs=(
            P("expert", None),
            P("expert", None),
            P("expert", None),
            P("expert", None),
            P("expert", "dp", None),
            P("expert", "dp", None),
            P("expert", "dp", None),
        ),
        out_specs=(
            P(("expert", "dp"), None),
            P(("expert", "dp"), None),
            P("expert", "dp", None),
            P("expert", "dp", None),
            P("expert", "dp", None),
        ),
        check_vma=False,
    )
```

```python
import jax
import jax.numpy as jnp
from jax import lax
from jax.sharding import PartitionSpec as P


def body(tokens, cotangent, route_ids, route_gates, w_gate, w_up, w_down):
    groups = lax.axis_size("expert")
    dp_count = lax.axis_size("dp")
    dp_idx = lax.axis_index("dp")
    tok_rows, width = tokens.shape
    top_slots = route_ids.shape[1]
    cap_rows = min(tok_rows, dp_count * max(1, tok_rows * top_slots * 5 // (4 * groups * dp_count)))
    share = cap_rows // dp_count
    n_dest = groups * share
    flat_ids = route_ids.reshape(-1)
    onehot = (flat_ids[:, None] == jnp.arange(groups, dtype=jnp.int32)[None, :]).astype(jnp.int32)
    slot_rank = jnp.sum(jnp.cumsum(onehot, axis=0) * onehot, axis=1) - 1
    local_rank = slot_rank - dp_idx * share
    mine = (local_rank >= 0) & (local_rank < share)
    dest = jnp.where(mine, local_rank * groups + flat_ids, n_dest)
    dest_hot = (dest[:, None] == jnp.arange(n_dest, dtype=jnp.int32)[None, :]).astype(jnp.float32)
    pick = jnp.sum(dest_hot.reshape(tok_rows, top_slots, n_dest), axis=1).T
    pick_bf = pick.astype(jnp.bfloat16)
    gate_sel = jnp.sum(dest_hot * route_gates.reshape(-1)[:, None], axis=0)
    send_x = jnp.dot(pick_bf, tokens, preferred_element_type=jnp.float32).astype(jnp.bfloat16)
    cot_sel = jnp.dot(pick_bf, cotangent, preferred_element_type=jnp.float32)
    send_dy = (gate_sel[:, None] * cot_sel).astype(jnp.bfloat16)

    def to_lanes(rows):
        return jnp.concatenate(
            [rows[r * groups : (r + 1) * groups] for r in range(share)], axis=1
        )

    def lanes_to_rows(packed):
        return jnp.concatenate(
            [packed[:, r * width : (r + 1) * width] for r in range(share)], axis=0
        )

    packed = jnp.concatenate([to_lanes(send_x), to_lanes(send_dy)], axis=1)
    recv = lax.all_to_all(packed, "expert", split_axis=0, concat_axis=0, tiled=True)
    gathered = lax.all_gather(recv, "dp", axis=0, tiled=True)
    half = share * width
    flat_x = lanes_to_rows(gathered[:, :half])
    flat_dy = lanes_to_rows(gathered[:, half:])
    gate_local = w_gate[0]
    up_local = w_up[0]
    down_local = w_down[0]
    by_feature = (((1,), (1,)), ((), ()))
    by_row = (((0,), (0,)), ((), ()))
    gate_pre = lax.dot_general(flat_x, gate_local, by_feature, preferred_element_type=jnp.float32)
    up_pre = lax.dot_general(flat_x, up_local, by_feature, preferred_element_type=jnp.float32)
    sigma_gate = jax.nn.sigmoid(gate_pre)
    hidden = (gate_pre * sigma_gate * up_pre).astype(jnp.bfloat16)
    y_part = jnp.dot(hidden, down_local, preferred_element_type=jnp.float32).astype(jnp.bfloat16)
    hidden_grad = lax.dot_general(
        flat_dy, down_local, by_feature, preferred_element_type=jnp.float32
    )
    grad_gate_pre = (
        hidden_grad * up_pre * sigma_gate * (1.0 + gate_pre * (1.0 - sigma_gate))
    ).astype(jnp.bfloat16)
    grad_up_pre = (hidden_grad * gate_pre * sigma_gate).astype(jnp.bfloat16)
    grad_down = lax.dot_general(hidden, flat_dy, by_row, preferred_element_type=jnp.float32)
    grad_gate = lax.dot_general(grad_gate_pre, flat_x, by_row, preferred_element_type=jnp.float32)
    grad_up = lax.dot_general(grad_up_pre, flat_x, by_row, preferred_element_type=jnp.float32)
    stack_rows = dp_count * groups
    y_lanes = jnp.concatenate(
        [y_part[r * stack_rows : (r + 1) * stack_rows] for r in range(share)], axis=1
    )
    y_sum = lax.psum_scatter(y_lanes, "dp", scatter_dimension=0, tiled=True)
    y_back = lax.all_to_all(y_sum, "expert", split_axis=0, concat_axis=0, tiled=True)
    y_home = lanes_to_rows(y_back).astype(jnp.float32)
    out_part = lax.dot_general(
        pick,
        gate_sel[:, None] * y_home,
        by_row,
        precision=lax.Precision.HIGHEST,
        preferred_element_type=jnp.float32,
    )
    dot_dest = jnp.sum(cot_sel * y_home, axis=1)
    dot_ext = jnp.concatenate([dot_dest, jnp.zeros((1,), jnp.float32)])
    grad_part = dot_ext[dest].reshape(tok_rows, top_slots)
    layer_sum = lax.psum_scatter(out_part, "dp", scatter_dimension=0, tiled=True)
    gate_sum = lax.psum_scatter(grad_part, "dp", scatter_dimension=0, tiled=True)
    return (
        layer_sum.astype(jnp.bfloat16),
        gate_sum,
        grad_gate.astype(jnp.bfloat16)[None],
        grad_up.astype(jnp.bfloat16)[None],
        grad_down.astype(jnp.bfloat16)[None],
    )


def solution(mesh):
    return jax.shard_map(
        body,
        mesh=mesh,
        in_specs=(
            P("expert", None),
            P("expert", None),
            P("expert", None),
            P("expert", None),
            P("expert", "dp", None),
            P("expert", "dp", None),
            P("expert", "dp", None),
        ),
        out_specs=(
            P(("expert", "dp"), None),
            P(("expert", "dp"), None),
            P("expert", "dp", None),
            P("expert", "dp", None),
            P("expert", "dp", None),
        ),
        check_vma=False,
    )
```

```python
import jax
import jax.numpy as jnp
from jax import lax
from jax.sharding import PartitionSpec as P


def body(tokens, cotangent, route_ids, route_gates, w_gate, w_up, w_down):
    groups = lax.axis_size("expert")
    dp_count = lax.axis_size("dp")
    dp_idx = lax.axis_index("dp")
    tok_rows, width = tokens.shape
    top_slots = route_ids.shape[1]
    cap_rows = min(tok_rows, dp_count * max(1, tok_rows * top_slots * 5 // (4 * groups * dp_count)))
    share = cap_rows // dp_count
    n_dest = groups * share
    flat_ids = route_ids.reshape(-1)
    onehot = (flat_ids[:, None] == jnp.arange(groups, dtype=jnp.int32)[None, :]).astype(jnp.int32)
    slot_rank = jnp.sum(jnp.cumsum(onehot, axis=0) * onehot, axis=1) - 1
    local_rank = slot_rank - dp_idx * share
    mine = (local_rank >= 0) & (local_rank < share)
    dest = jnp.where(mine, local_rank * groups + flat_ids, n_dest)
    dest_hot = (dest[:, None] == jnp.arange(n_dest, dtype=jnp.int32)[None, :]).astype(jnp.float32)
    pick = jnp.sum(dest_hot.reshape(tok_rows, top_slots, n_dest), axis=1).T
    pick_bf = pick.astype(jnp.bfloat16)
    gate_sel = jnp.sum(dest_hot * route_gates.reshape(-1)[:, None], axis=0)
    send_x = jnp.dot(pick_bf, tokens, preferred_element_type=jnp.float32).astype(jnp.bfloat16)
    cot_sel = jnp.dot(pick_bf, cotangent, preferred_element_type=jnp.float32)
    send_dy = (gate_sel[:, None] * cot_sel).astype(jnp.bfloat16)

    def to_lanes(rows):
        return jnp.concatenate(
            [rows[r * groups : (r + 1) * groups] for r in range(share)], axis=1
        )

    def lanes_to_rows(packed):
        return jnp.concatenate(
            [packed[:, r * width : (r + 1) * width] for r in range(share)], axis=0
        )

    recv_x = lax.all_to_all(to_lanes(send_x), "expert", split_axis=0, concat_axis=0, tiled=True)
    recv_x, lanes_dy = lax.optimization_barrier((recv_x, to_lanes(send_dy)))
    recv_dy = lax.all_to_all(lanes_dy, "expert", split_axis=0, concat_axis=0, tiled=True)
    flat_x = lanes_to_rows(lax.all_gather(recv_x, "dp", axis=0, tiled=True))
    flat_dy = lanes_to_rows(lax.all_gather(recv_dy, "dp", axis=0, tiled=True))
    gate_local = w_gate[0]
    up_local = w_up[0]
    down_local = w_down[0]
    by_feature = (((1,), (1,)), ((), ()))
    by_row = (((0,), (0,)), ((), ()))
    gate_pre = lax.dot_general(flat_x, gate_local, by_feature, preferred_element_type=jnp.float32)
    up_pre = lax.dot_general(flat_x, up_local, by_feature, preferred_element_type=jnp.float32)
    sigma_gate = jax.nn.sigmoid(gate_pre)
    hidden = (gate_pre * sigma_gate * up_pre).astype(jnp.bfloat16)
    y_part = jnp.dot(hidden, down_local, preferred_element_type=jnp.float32).astype(jnp.bfloat16)
    hidden_grad = lax.dot_general(
        flat_dy, down_local, by_feature, preferred_element_type=jnp.float32
    )
    grad_gate_pre = (
        hidden_grad * up_pre * sigma_gate * (1.0 + gate_pre * (1.0 - sigma_gate))
    ).astype(jnp.bfloat16)
    grad_up_pre = (hidden_grad * gate_pre * sigma_gate).astype(jnp.bfloat16)
    grad_down = lax.dot_general(hidden, flat_dy, by_row, preferred_element_type=jnp.float32)
    grad_gate = lax.dot_general(grad_gate_pre, flat_x, by_row, preferred_element_type=jnp.float32)
    grad_up = lax.dot_general(grad_up_pre, flat_x, by_row, preferred_element_type=jnp.float32)
    stack_rows = dp_count * groups
    y_lanes = jnp.concatenate(
        [y_part[r * stack_rows : (r + 1) * stack_rows] for r in range(share)], axis=1
    )
    y_sum = lax.psum_scatter(y_lanes, "dp", scatter_dimension=0, tiled=True)
    y_sum, grad_gate, grad_up, grad_down = lax.optimization_barrier(
        (y_sum, grad_gate, grad_up, grad_down)
    )
    y_back = lax.all_to_all(y_sum, "expert", split_axis=0, concat_axis=0, tiled=True)
    y_home = lanes_to_rows(y_back).astype(jnp.float32)
    out_part = lax.dot_general(
        pick,
        gate_sel[:, None] * y_home,
        by_row,
        precision=lax.Precision.HIGHEST,
        preferred_element_type=jnp.float32,
    )
    dot_dest = jnp.sum(cot_sel * y_home, axis=1)
    dot_ext = jnp.concatenate([dot_dest, jnp.zeros((1,), jnp.float32)])
    grad_part = dot_ext[dest].reshape(tok_rows, top_slots)
    layer_sum = lax.psum_scatter(out_part, "dp", scatter_dimension=0, tiled=True)
    gate_sum = lax.psum_scatter(grad_part, "dp", scatter_dimension=0, tiled=True)
    return (
        layer_sum.astype(jnp.bfloat16),
        gate_sum,
        grad_gate.astype(jnp.bfloat16)[None],
        grad_up.astype(jnp.bfloat16)[None],
        grad_down.astype(jnp.bfloat16)[None],
    )


def solution(mesh):
    return jax.shard_map(
        body,
        mesh=mesh,
        in_specs=(
            P("expert", None),
            P("expert", None),
            P("expert", None),
            P("expert", None),
            P("expert", "dp", None),
            P("expert", "dp", None),
            P("expert", "dp", None),
        ),
        out_specs=(
            P(("expert", "dp"), None),
            P(("expert", "dp"), None),
            P("expert", "dp", None),
            P("expert", "dp", None),
            P("expert", "dp", None),
        ),
        check_vma=False,
    )
```

```python
import jax
import jax.numpy as jnp
from jax import lax
from jax.sharding import PartitionSpec as P


def body(tokens, cotangent, route_ids, route_gates, w_gate, w_up, w_down):
    groups = lax.axis_size("expert")
    dp_count = lax.axis_size("dp")
    dp_idx = lax.axis_index("dp")
    tok_rows, width = tokens.shape
    top_slots = route_ids.shape[1]
    cap_rows = min(tok_rows, dp_count * max(1, tok_rows * top_slots * 5 // (4 * groups * dp_count)))
    share = cap_rows // dp_count
    n_dest = groups * share
    flat_ids = route_ids.reshape(-1)
    onehot = (flat_ids[:, None] == jnp.arange(groups, dtype=jnp.int32)[None, :]).astype(jnp.int32)
    n_slots = flat_ids.shape[0]
    lower = (
        jnp.arange(n_slots, dtype=jnp.int32)[:, None] >= jnp.arange(n_slots, dtype=jnp.int32)[None, :]
    ).astype(jnp.bfloat16)
    running = jnp.dot(lower, onehot.astype(jnp.bfloat16), preferred_element_type=jnp.float32)
    slot_rank = jnp.sum(running.astype(jnp.int32) * onehot, axis=1) - 1
    local_rank = slot_rank - dp_idx * share
    mine = (local_rank >= 0) & (local_rank < share)
    dest = jnp.where(mine, local_rank * groups + flat_ids, n_dest)
    dest_hot = (dest[:, None] == jnp.arange(n_dest, dtype=jnp.int32)[None, :]).astype(jnp.float32)
    pick = jnp.sum(dest_hot.reshape(tok_rows, top_slots, n_dest), axis=1).T
    pick_bf = pick.astype(jnp.bfloat16)
    gate_sel = jnp.sum(dest_hot * route_gates.reshape(-1)[:, None], axis=0)
    send_x = jnp.dot(pick_bf, tokens, preferred_element_type=jnp.float32).astype(jnp.bfloat16)
    cot_sel = jnp.dot(pick_bf, cotangent, preferred_element_type=jnp.float32)
    send_dy = (gate_sel[:, None] * cot_sel).astype(jnp.bfloat16)

    def to_lanes(rows):
        return jnp.concatenate(
            [rows[r * groups : (r + 1) * groups] for r in range(share)], axis=1
        )

    def lanes_to_rows(packed):
        return jnp.concatenate(
            [packed[:, r * width : (r + 1) * width] for r in range(share)], axis=0
        )

    recv_x = lax.all_to_all(to_lanes(send_x), "expert", split_axis=0, concat_axis=0, tiled=True)
    recv_x, lanes_dy = lax.optimization_barrier((recv_x, to_lanes(send_dy)))
    recv_dy = lax.all_to_all(lanes_dy, "expert", split_axis=0, concat_axis=0, tiled=True)
    flat_x = lanes_to_rows(lax.all_gather(recv_x, "dp", axis=0, tiled=True))
    flat_dy = lanes_to_rows(lax.all_gather(recv_dy, "dp", axis=0, tiled=True))
    gate_local = w_gate[0]
    up_local = w_up[0]
    down_local = w_down[0]
    by_feature = (((1,), (1,)), ((), ()))
    by_row = (((0,), (0,)), ((), ()))
    gate_pre = lax.dot_general(flat_x, gate_local, by_feature, preferred_element_type=jnp.float32)
    up_pre = lax.dot_general(flat_x, up_local, by_feature, preferred_element_type=jnp.float32)
    sigma_gate = jax.nn.sigmoid(gate_pre)
    hidden = (gate_pre * sigma_gate * up_pre).astype(jnp.bfloat16)
    y_part = jnp.dot(hidden, down_local, preferred_element_type=jnp.float32).astype(jnp.bfloat16)
    hidden_grad = lax.dot_general(
        flat_dy, down_local, by_feature, preferred_element_type=jnp.float32
    )
    grad_gate_pre = (
        hidden_grad * up_pre * sigma_gate * (1.0 + gate_pre * (1.0 - sigma_gate))
    ).astype(jnp.bfloat16)
    grad_up_pre = (hidden_grad * gate_pre * sigma_gate).astype(jnp.bfloat16)
    grad_down = lax.dot_general(hidden, flat_dy, by_row, preferred_element_type=jnp.float32)
    grad_gate = lax.dot_general(grad_gate_pre, flat_x, by_row, preferred_element_type=jnp.float32)
    grad_up = lax.dot_general(grad_up_pre, flat_x, by_row, preferred_element_type=jnp.float32)
    stack_rows = dp_count * groups
    y_lanes = jnp.concatenate(
        [y_part[r * stack_rows : (r + 1) * stack_rows] for r in range(share)], axis=1
    )
    y_sum = lax.psum_scatter(y_lanes, "dp", scatter_dimension=0, tiled=True)
    y_sum, grad_gate, grad_up, grad_down = lax.optimization_barrier(
        (y_sum, grad_gate, grad_up, grad_down)
    )
    y_back = lax.all_to_all(y_sum, "expert", split_axis=0, concat_axis=0, tiled=True)
    y_home = lanes_to_rows(y_back).astype(jnp.float32)
    out_part = lax.dot_general(
        pick,
        gate_sel[:, None] * y_home,
        by_row,
        precision=lax.Precision.HIGHEST,
        preferred_element_type=jnp.float32,
    )
    dot_dest = jnp.sum(cot_sel * y_home, axis=1)
    dot_ext = jnp.concatenate([dot_dest, jnp.zeros((1,), jnp.float32)])
    grad_part = dot_ext[dest].reshape(tok_rows, top_slots)
    both_sum = lax.psum_scatter(
        jnp.concatenate([out_part, grad_part], axis=1), "dp", scatter_dimension=0, tiled=True
    )
    layer_sum = both_sum[:, :width]
    gate_sum = both_sum[:, width:]
    return (
        layer_sum.astype(jnp.bfloat16),
        gate_sum,
        grad_gate.astype(jnp.bfloat16)[None],
        grad_up.astype(jnp.bfloat16)[None],
        grad_down.astype(jnp.bfloat16)[None],
    )


def solution(mesh):
    return jax.shard_map(
        body,
        mesh=mesh,
        in_specs=(
            P("expert", None),
            P("expert", None),
            P("expert", None),
            P("expert", None),
            P("expert", "dp", None),
            P("expert", "dp", None),
            P("expert", "dp", None),
        ),
        out_specs=(
            P(("expert", "dp"), None),
            P(("expert", "dp"), None),
            P("expert", "dp", None),
            P("expert", "dp", None),
            P("expert", "dp", None),
        ),
        check_vma=False,
    )
```

```python
import jax
import jax.numpy as jnp
from jax import lax
from jax.sharding import PartitionSpec as P


def body(tokens, cotangent, route_ids, route_gates, w_gate, w_up, w_down):
    groups = lax.axis_size("expert")
    dp_count = lax.axis_size("dp")
    dp_idx = lax.axis_index("dp")
    tok_rows, width = tokens.shape
    top_slots = route_ids.shape[1]
    cap_rows = min(tok_rows, dp_count * max(1, tok_rows * top_slots * 5 // (4 * groups * dp_count)))
    share = cap_rows // dp_count
    n_dest = groups * share
    flat_ids = route_ids.reshape(-1)
    onehot = (flat_ids[:, None] == jnp.arange(groups, dtype=jnp.int32)[None, :]).astype(jnp.int32)
    n_slots = flat_ids.shape[0]
    lower = (
        jnp.arange(n_slots, dtype=jnp.int32)[:, None] >= jnp.arange(n_slots, dtype=jnp.int32)[None, :]
    ).astype(jnp.bfloat16)
    running = jnp.dot(lower, onehot.astype(jnp.bfloat16), preferred_element_type=jnp.float32)
    slot_rank = jnp.sum(running.astype(jnp.int32) * onehot, axis=1) - 1
    local_rank = slot_rank - dp_idx * share
    mine = (local_rank >= 0) & (local_rank < share)
    dest = jnp.where(mine, local_rank * groups + flat_ids, n_dest)
    dest_hot = (dest[:, None] == jnp.arange(n_dest, dtype=jnp.int32)[None, :]).astype(jnp.float32)
    pick = jnp.sum(dest_hot.reshape(tok_rows, top_slots, n_dest), axis=1).T
    pick_bf = pick.astype(jnp.bfloat16)
    gate_sel = jnp.sum(dest_hot * route_gates.reshape(-1)[:, None], axis=0)
    send_x = jnp.dot(pick_bf, tokens, preferred_element_type=jnp.float32).astype(jnp.bfloat16)
    cot_sel = jnp.dot(pick_bf, cotangent, preferred_element_type=jnp.float32)
    send_dy = (gate_sel[:, None] * cot_sel).astype(jnp.bfloat16)

    def to_lanes(rows):
        return jnp.concatenate(
            [rows[r * groups : (r + 1) * groups] for r in range(share)], axis=1
        )

    def lanes_to_rows(packed):
        return jnp.concatenate(
            [packed[:, r * width : (r + 1) * width] for r in range(share)], axis=0
        )

    recv_x = lax.all_to_all(to_lanes(send_x), "expert", split_axis=0, concat_axis=0, tiled=True)
    recv_x, lanes_dy = lax.optimization_barrier((recv_x, to_lanes(send_dy)))
    recv_dy = lax.all_to_all(lanes_dy, "expert", split_axis=0, concat_axis=0, tiled=True)
    flat_x = lanes_to_rows(lax.all_gather(recv_x, "dp", axis=0, tiled=True))
    gate_local = w_gate[0]
    up_local = w_up[0]
    down_local = w_down[0]
    by_feature = (((1,), (1,)), ((), ()))
    by_row = (((0,), (0,)), ((), ()))
    gate_pre = lax.dot_general(flat_x, gate_local, by_feature, preferred_element_type=jnp.float32)
    up_pre = lax.dot_general(flat_x, up_local, by_feature, preferred_element_type=jnp.float32)
    sigma_gate = jax.nn.sigmoid(gate_pre)
    hidden = (gate_pre * sigma_gate * up_pre).astype(jnp.bfloat16)
    y_part = jnp.dot(hidden, down_local, preferred_element_type=jnp.float32).astype(jnp.bfloat16)
    stack_rows = dp_count * groups
    y_lanes = jnp.concatenate(
        [y_part[r * stack_rows : (r + 1) * stack_rows] for r in range(share)], axis=1
    )
    y_sum = lax.psum_scatter(y_lanes, "dp", scatter_dimension=0, tiled=True)
    y_sum, recv_dy = lax.optimization_barrier((y_sum, recv_dy))
    flat_dy = lanes_to_rows(lax.all_gather(recv_dy, "dp", axis=0, tiled=True))
    y_back = lax.all_to_all(y_sum, "expert", split_axis=0, concat_axis=0, tiled=True)
    y_back, flat_dy = lax.optimization_barrier((y_back, flat_dy))
    y_home = lanes_to_rows(y_back).astype(jnp.float32)
    hidden_grad = lax.dot_general(
        flat_dy, down_local, by_feature, preferred_element_type=jnp.float32
    )
    grad_gate_pre = (
        hidden_grad * up_pre * sigma_gate * (1.0 + gate_pre * (1.0 - sigma_gate))
    ).astype(jnp.bfloat16)
    grad_up_pre = (hidden_grad * gate_pre * sigma_gate).astype(jnp.bfloat16)
    grad_down = lax.dot_general(hidden, flat_dy, by_row, preferred_element_type=jnp.float32)
    grad_gate = lax.dot_general(grad_gate_pre, flat_x, by_row, preferred_element_type=jnp.float32)
    grad_up = lax.dot_general(grad_up_pre, flat_x, by_row, preferred_element_type=jnp.float32)
    out_part = lax.dot_general(
        pick,
        gate_sel[:, None] * y_home,
        by_row,
        precision=lax.Precision.HIGHEST,
        preferred_element_type=jnp.float32,
    )
    dot_dest = jnp.sum(cot_sel * y_home, axis=1)
    grad_part = jnp.sum(dest_hot * dot_dest[None, :], axis=1).reshape(tok_rows, top_slots)
    both_sum = lax.psum_scatter(
        jnp.concatenate([out_part, grad_part], axis=1), "dp", scatter_dimension=0, tiled=True
    )
    layer_sum = both_sum[:, :width]
    gate_sum = both_sum[:, width:]
    return (
        layer_sum.astype(jnp.bfloat16),
        gate_sum,
        grad_gate.astype(jnp.bfloat16)[None],
        grad_up.astype(jnp.bfloat16)[None],
        grad_down.astype(jnp.bfloat16)[None],
    )


def solution(mesh):
    return jax.shard_map(
        body,
        mesh=mesh,
        in_specs=(
            P("expert", None),
            P("expert", None),
            P("expert", None),
            P("expert", None),
            P("expert", "dp", None),
            P("expert", "dp", None),
            P("expert", "dp", None),
        ),
        out_specs=(
            P(("expert", "dp"), None),
            P(("expert", "dp"), None),
            P("expert", "dp", None),
            P("expert", "dp", None),
            P("expert", "dp", None),
        ),
        check_vma=False,
    )
```

```python
import jax
import jax.numpy as jnp
from jax import lax
from jax.sharding import PartitionSpec as P


def body(tokens, cotangent, route_ids, route_gates, w_gate, w_up, w_down):
    groups = lax.axis_size("expert")
    dp_count = lax.axis_size("dp")
    dp_idx = lax.axis_index("dp")
    tok_rows, width = tokens.shape
    top_slots = route_ids.shape[1]
    cap_rows = min(tok_rows, dp_count * max(1, tok_rows * top_slots * 5 // (4 * groups * dp_count)))
    share = cap_rows // dp_count
    n_dest = groups * share
    flat_ids = route_ids.reshape(-1)
    onehot = (flat_ids[:, None] == jnp.arange(groups, dtype=jnp.int32)[None, :]).astype(jnp.int32)
    n_slots = flat_ids.shape[0]
    lower = (
        jnp.arange(n_slots, dtype=jnp.int32)[:, None] >= jnp.arange(n_slots, dtype=jnp.int32)[None, :]
    ).astype(jnp.bfloat16)
    running = jnp.dot(lower, onehot.astype(jnp.bfloat16), preferred_element_type=jnp.float32)
    slot_rank = jnp.sum(running.astype(jnp.int32) * onehot, axis=1) - 1
    local_rank = slot_rank - dp_idx * share
    mine = (local_rank >= 0) & (local_rank < share)
    dest = jnp.where(mine, local_rank * groups + flat_ids, n_dest)
    dest_hot = (dest[:, None] == jnp.arange(n_dest, dtype=jnp.int32)[None, :]).astype(jnp.float32)
    pick = jnp.sum(dest_hot.reshape(tok_rows, top_slots, n_dest), axis=1).T
    pick_bf = pick.astype(jnp.bfloat16)
    gate_sel = jnp.sum(dest_hot * route_gates.reshape(-1)[:, None], axis=0)
    send_x = jnp.dot(pick_bf, tokens, preferred_element_type=jnp.float32).astype(jnp.bfloat16)
    cot_sel = jnp.dot(pick_bf, cotangent, preferred_element_type=jnp.float32)
    send_dy = (gate_sel[:, None] * cot_sel).astype(jnp.bfloat16)

    def to_lanes(rows):
        return jnp.concatenate(
            [rows[r * groups : (r + 1) * groups] for r in range(share)], axis=1
        )

    def lanes_to_rows(packed):
        return jnp.concatenate(
            [packed[:, r * width : (r + 1) * width] for r in range(share)], axis=0
        )

    recv_x = lax.all_to_all(to_lanes(send_x), "expert", split_axis=0, concat_axis=0, tiled=True)
    recv_x, lanes_dy = lax.optimization_barrier((recv_x, to_lanes(send_dy)))
    recv_dy = lax.all_to_all(lanes_dy, "expert", split_axis=0, concat_axis=0, tiled=True)
    flat_x = lanes_to_rows(lax.all_gather(recv_x, "dp", axis=0, tiled=True))
    gate_local = w_gate[0]
    up_local = w_up[0]
    down_local = w_down[0]
    by_feature = (((1,), (1,)), ((), ()))
    by_row = (((0,), (0,)), ((), ()))
    gate_pre = lax.dot_general(flat_x, gate_local, by_feature, preferred_element_type=jnp.float32)
    up_pre = lax.dot_general(flat_x, up_local, by_feature, preferred_element_type=jnp.float32)
    sigma_gate = jax.nn.sigmoid(gate_pre)
    hidden = (gate_pre * sigma_gate * up_pre).astype(jnp.bfloat16)
    y_part = jnp.dot(hidden, down_local, preferred_element_type=jnp.float32).astype(jnp.bfloat16)
    stack_rows = dp_count * groups
    y_lanes = jnp.concatenate(
        [y_part[r * stack_rows : (r + 1) * stack_rows] for r in range(share)], axis=1
    )
    y_sum = lax.psum_scatter(y_lanes, "dp", scatter_dimension=0, tiled=True)
    y_sum, recv_dy = lax.optimization_barrier((y_sum, recv_dy))
    flat_dy = lanes_to_rows(lax.all_gather(recv_dy, "dp", axis=0, tiled=True))
    y_back = lax.all_to_all(y_sum, "expert", split_axis=0, concat_axis=0, tiled=True)
    y_back, flat_dy = lax.optimization_barrier((y_back, flat_dy))
    y_home = lanes_to_rows(y_back).astype(jnp.float32)
    hidden_grad = lax.dot_general(
        flat_dy, down_local, by_feature, preferred_element_type=jnp.float32
    )
    grad_gate_pre = (
        hidden_grad * up_pre * sigma_gate * (1.0 + gate_pre * (1.0 - sigma_gate))
    ).astype(jnp.bfloat16)
    grad_up_pre = (hidden_grad * gate_pre * sigma_gate).astype(jnp.bfloat16)
    grad_down = lax.dot_general(hidden, flat_dy, by_row, preferred_element_type=jnp.float32)
    grad_gate = lax.dot_general(grad_gate_pre, flat_x, by_row, preferred_element_type=jnp.float32)
    grad_up = lax.dot_general(grad_up_pre, flat_x, by_row, preferred_element_type=jnp.float32)
    out_part = lax.dot_general(
        pick,
        gate_sel[:, None] * y_home,
        by_row,
        precision=lax.Precision.HIGHEST,
        preferred_element_type=jnp.float32,
    )
    dot_dest = jnp.sum(cot_sel * y_home, axis=1)
    grad_part = jnp.sum(dest_hot * dot_dest[None, :], axis=1).reshape(tok_rows, top_slots)
    both_sum = lax.psum_scatter(
        jnp.concatenate([out_part, grad_part], axis=1).astype(jnp.bfloat16),
        "dp",
        scatter_dimension=0,
        tiled=True,
    )
    layer_sum = both_sum[:, :width]
    gate_sum = both_sum[:, width:].astype(jnp.float32)
    return (
        layer_sum.astype(jnp.bfloat16),
        gate_sum,
        grad_gate.astype(jnp.bfloat16)[None],
        grad_up.astype(jnp.bfloat16)[None],
        grad_down.astype(jnp.bfloat16)[None],
    )


def solution(mesh):
    return jax.shard_map(
        body,
        mesh=mesh,
        in_specs=(
            P("expert", None),
            P("expert", None),
            P("expert", None),
            P("expert", None),
            P("expert", "dp", None),
            P("expert", "dp", None),
            P("expert", "dp", None),
        ),
        out_specs=(
            P(("expert", "dp"), None),
            P(("expert", "dp"), None),
            P("expert", "dp", None),
            P("expert", "dp", None),
            P("expert", "dp", None),
        ),
        check_vma=False,
    )
```

```python
import jax
import jax.numpy as jnp
from jax import lax
from jax.sharding import PartitionSpec as P


def body(tokens, cotangent, route_ids, route_gates, w_gate, w_up, w_down):
    groups = lax.axis_size("expert")
    dp_count = lax.axis_size("dp")
    dp_idx = lax.axis_index("dp")
    tok_rows, width = tokens.shape
    top_slots = route_ids.shape[1]
    cap_rows = min(tok_rows, dp_count * max(1, tok_rows * top_slots * 5 // (4 * groups * dp_count)))
    share = cap_rows // dp_count
    n_dest = groups * share
    flat_ids = route_ids.reshape(-1)
    onehot = (flat_ids[:, None] == jnp.arange(groups, dtype=jnp.int32)[None, :]).astype(jnp.int32)
    n_slots = flat_ids.shape[0]
    lower = (
        jnp.arange(n_slots, dtype=jnp.int32)[:, None] >= jnp.arange(n_slots, dtype=jnp.int32)[None, :]
    ).astype(jnp.bfloat16)
    running = jnp.dot(lower, onehot.astype(jnp.bfloat16), preferred_element_type=jnp.float32)
    slot_rank = jnp.sum(running.astype(jnp.int32) * onehot, axis=1) - 1
    local_rank = slot_rank - dp_idx * share
    mine = (local_rank >= 0) & (local_rank < share)
    dest = jnp.where(mine, local_rank * groups + flat_ids, n_dest)
    dest_hot = (dest[:, None] == jnp.arange(n_dest, dtype=jnp.int32)[None, :]).astype(jnp.float32)
    pick = jnp.sum(dest_hot.reshape(tok_rows, top_slots, n_dest), axis=1).T
    pick_bf = pick.astype(jnp.bfloat16)
    gate_sel = jnp.sum(dest_hot * route_gates.reshape(-1)[:, None], axis=0)
    send_x = jnp.dot(pick_bf, tokens, preferred_element_type=jnp.float32).astype(jnp.bfloat16)
    cot_sel = jnp.dot(pick_bf, cotangent, preferred_element_type=jnp.float32)
    send_dy = (gate_sel[:, None] * cot_sel).astype(jnp.bfloat16)

    def to_lanes(rows):
        return jnp.concatenate(
            [rows[r * groups : (r + 1) * groups] for r in range(share)], axis=1
        )

    def lanes_to_rows(packed):
        return jnp.concatenate(
            [packed[:, r * width : (r + 1) * width] for r in range(share)], axis=0
        )

    recv_x = lax.all_to_all(to_lanes(send_x), "expert", split_axis=0, concat_axis=0, tiled=True)
    recv_x, lanes_dy = lax.optimization_barrier((recv_x, to_lanes(send_dy)))
    recv_dy = lax.all_to_all(lanes_dy, "expert", split_axis=0, concat_axis=0, tiled=True)
    gathered_x = lax.all_gather(recv_x, "dp", axis=0, tiled=True)
    x_chunks = [gathered_x[:, r * width : (r + 1) * width] for r in range(share)]
    gate_local = w_gate[0]
    up_local = w_up[0]
    down_local = w_down[0]
    by_feature = (((1,), (1,)), ((), ()))
    by_row = (((0,), (0,)), ((), ()))
    gate_pre = jnp.concatenate(
        [
            lax.dot_general(xc, gate_local, by_feature, preferred_element_type=jnp.float32)
            for xc in x_chunks
        ],
        axis=0,
    )
    up_pre = jnp.concatenate(
        [
            lax.dot_general(xc, up_local, by_feature, preferred_element_type=jnp.float32)
            for xc in x_chunks
        ],
        axis=0,
    )
    sigma_gate = jax.nn.sigmoid(gate_pre)
    hidden = (gate_pre * sigma_gate * up_pre).astype(jnp.bfloat16)
    stack_rows = dp_count * groups
    y_lanes = jnp.concatenate(
        [
            jnp.dot(
                hidden[r * stack_rows : (r + 1) * stack_rows],
                down_local,
                preferred_element_type=jnp.float32,
            ).astype(jnp.bfloat16)
            for r in range(share)
        ],
        axis=1,
    )
    flat_x = jnp.concatenate(x_chunks, axis=0)
    y_sum = lax.psum_scatter(y_lanes, "dp", scatter_dimension=0, tiled=True)
    y_sum, recv_dy = lax.optimization_barrier((y_sum, recv_dy))
    flat_dy = lanes_to_rows(lax.all_gather(recv_dy, "dp", axis=0, tiled=True))
    y_back = lax.all_to_all(y_sum, "expert", split_axis=0, concat_axis=0, tiled=True)
    y_back, flat_dy = lax.optimization_barrier((y_back, flat_dy))
    y_home = lanes_to_rows(y_back).astype(jnp.float32)
    hidden_grad = lax.dot_general(
        flat_dy, down_local, by_feature, preferred_element_type=jnp.float32
    )
    grad_gate_pre = (
        hidden_grad * up_pre * sigma_gate * (1.0 + gate_pre * (1.0 - sigma_gate))
    ).astype(jnp.bfloat16)
    grad_up_pre = (hidden_grad * gate_pre * sigma_gate).astype(jnp.bfloat16)
    grad_down = lax.dot_general(hidden, flat_dy, by_row, preferred_element_type=jnp.float32)
    grad_gate = lax.dot_general(grad_gate_pre, flat_x, by_row, preferred_element_type=jnp.float32)
    grad_up = lax.dot_general(grad_up_pre, flat_x, by_row, preferred_element_type=jnp.float32)
    out_part = lax.dot_general(
        pick,
        gate_sel[:, None] * y_home,
        by_row,
        precision=lax.Precision.HIGHEST,
        preferred_element_type=jnp.float32,
    )
    dot_dest = jnp.sum(cot_sel * y_home, axis=1)
    grad_part = jnp.sum(dest_hot * dot_dest[None, :], axis=1).reshape(tok_rows, top_slots)
    both_sum = lax.psum_scatter(
        jnp.concatenate([out_part, grad_part], axis=1).astype(jnp.bfloat16),
        "dp",
        scatter_dimension=0,
        tiled=True,
    )
    layer_sum = both_sum[:, :width]
    gate_sum = both_sum[:, width:].astype(jnp.float32)
    return (
        layer_sum.astype(jnp.bfloat16),
        gate_sum,
        grad_gate.astype(jnp.bfloat16)[None],
        grad_up.astype(jnp.bfloat16)[None],
        grad_down.astype(jnp.bfloat16)[None],
    )


def solution(mesh):
    return jax.shard_map(
        body,
        mesh=mesh,
        in_specs=(
            P("expert", None),
            P("expert", None),
            P("expert", None),
            P("expert", None),
            P("expert", "dp", None),
            P("expert", "dp", None),
            P("expert", "dp", None),
        ),
        out_specs=(
            P(("expert", "dp"), None),
            P(("expert", "dp"), None),
            P("expert", "dp", None),
            P("expert", "dp", None),
            P("expert", "dp", None),
        ),
        check_vma=False,
    )
```
